256 devices in a mesh: ctx: 8 (over y, x_hi), ch: 32 (over z, x_lo, core).
Axes of the slice: x: 4 (x_hi: 2, x_lo: 2; x = x_hi * 2 + x_lo), y: 4, z: 8, core: 2. Of those that a mesh axis runs over, the one named last changes fastest.
Arguments:
- gate_act: bfloat16 [4096, 8192], P('ctx', 'ch'), may hold values from -6 to 6
- key_act: bfloat16 [4096, 8192], P('ctx', 'ch'), may hold values from -6 to 6
- value_act: bfloat16 [4096, 8192], P('ctx', 'ch'), may hold values from -6 to 6
- filter_taps: float32 [6144, 8192], P('ctx', 'ch'), may hold values from -2 to 2
- skip_gain: float32 [8192], P('ch'), may hold values from 0.5 to 1.5
- w_out: bfloat16 [8192, 8192], P(None, 'ch'), may hold values from -0.0625 to 0.0625
- span_order: int32 [16], replicated, may hold values from 0 to 15, each once
- decode_order: int32 [8], replicated, may hold values from 0 to 7, each once
Outputs:
- projected: bfloat16 [4096, 8192], P('ctx', 'ch')
- tail: float32 [2048, 8192], P('ctx', 'ch')
The draws below stay inside these ranges and needn't reach their ends.
Inputs may be any that keep to these rules, and one draw needn't show every extreme that they name: `span_order`: each span number once. `decode_order`: each future block number once.
All inputs are finite; a program needn't handle non-finite values.
Results may differ from the reference program's by a relative error of at most 0.017.
Values may be sent and summed in bfloat16 or wider, within the bound.
No kernel may reach another device: no remote copies, remote signals or barrier semaphores. Data moves between devices by JAX's collectives and lax.ppermute only.
A program may use at most 128 MiB of HBM per device.

```python
import math
import jax
import jax.numpy as jnp
from jax import lax

D = 8192
SPAN = 256
SPANS = 16
TOKENS = 4096
FUT_BLOCKS = 8
FUTURE = 2048
LAGS = 24


def draw_filter_taps(key, part):
    random_subkeys = jax.random.split(key, 7)
    grand_total = LAGS * SPAN
    lag_dimension = jnp.arange(grand_total, dtype=jnp.float32)[:, None]
    fast_share = 0.4
    slow_low = math.log(0.25 * grand_total)
    slow_high = math.log(4.0 * grand_total)
    is_fast = jax.random.uniform(random_subkeys[0], (1, D)) < fast_share
    quick_rate = jnp.exp(jax.random.uniform(random_subkeys[1], (1, D), minval=math.log(30.0), maxval=math.log(50.0)))
    slow_rate = jnp.exp(jax.random.uniform(random_subkeys[2], (1, D), minval=slow_low, maxval=slow_high))
    decay_len = jnp.where(is_fast, quick_rate, slow_rate)
    filter_envelope = jnp.exp(-lag_dimension / decay_len)
    spike_location = jax.random.randint(random_subkeys[3], (3,), 1, grand_total)
    spike_retained = jax.random.uniform(random_subkeys[4], (3,), minval=0.5, maxval=0.8)
    for spike_pulse in range(3):
        filter_envelope = filter_envelope * jnp.where(lag_dimension >= spike_location[spike_pulse].astype(jnp.float32), spike_retained[spike_pulse], 1.0)
    amplitude = jnp.sqrt(1.0 / jnp.minimum(0.5 * decay_len, float(grand_total)))
    rough_part = jnp.clip(jax.random.normal(random_subkeys[6], (grand_total, D)), -6.0, 6.0)
    return (amplitude * filter_envelope * rough_part).astype(jnp.float32)


def block_levels(stream_key, shape, cuts, smallest, largest):
    gain = 1.0
    for position, blocks in cuts:
        steps = jax.random.uniform(jax.random.fold_in(jax.random.fold_in(stream_key, 6), position), (blocks,), jnp.float32, smallest / len(cuts), largest / len(cuts))
        gain = gain * jnp.repeat(jnp.exp(steps), shape[position] // blocks).reshape((-1,) + (1,) * (len(shape) - 1 - position))
    return gain


def normal_values(stream_key, dims, spread, bound, cuts=(), kind=jnp.bfloat16):
    values = jax.random.normal(stream_key, dims, jnp.float32) * spread
    if len(cuts) > 0:
        values = block_levels(stream_key, dims, cuts, -0.22, 0.18) * values
    return jnp.clip(values, min=-bound, max=bound).astype(kind)


def setup_inputs(seed: int = 0) -> dict:
    keys = jax.random.split(jax.random.key(seed), 9)
    gate_act = normal_values(keys[0], (TOKENS, D), 1.0, 6.0, ((0, 8), (1, 32)))
    key_act = normal_values(keys[1], (TOKENS, D), 1.0, 6.0, ((0, 8), (1, 32)))
    value_act = normal_values(keys[2], (TOKENS, D), 1.0, 6.0, ((0, 8), (1, 32)))
    filter_taps = draw_filter_taps(jax.random.fold_in(keys[8], 71), 0)
    skip_gain = jnp.clip(0.5 + 1.0 * jax.random.uniform(keys[4], (D,), jnp.float32) ** block_levels(keys[4], (D,), ((0, 32),), -0.2, 0.2), 0.5, 1.5)
    w_out = normal_values(keys[5], (D, D), D ** -0.5, 0.0625, ((1, 32),))
    span_order = jax.random.permutation(keys[6], SPANS).astype(jnp.int32)
    decode_order = jax.random.permutation(keys[7], FUT_BLOCKS).astype(jnp.int32)
    return {"gate_act": gate_act, "key_act": key_act, "value_act": value_act, "filter_taps": filter_taps, "skip_gain": skip_gain, "w_out": w_out, "span_order": span_order, "decode_order": decode_order}


def reference(gate_act, key_act, value_act, filter_taps, skip_gain, w_out, span_order, decode_order):
    signal = (key_act.astype(jnp.float32) * value_act.astype(jnp.float32)).astype(jnp.bfloat16)
    slot_of = jnp.zeros((SPANS,), jnp.int32).at[span_order].set(jnp.arange(SPANS, dtype=jnp.int32))
    natural = signal.reshape(SPANS, SPAN, D)[slot_of].reshape(TOKENS, D).astype(jnp.float32)
    extent = TOKENS + FUTURE
    fft_len = 1 << (TOKENS + LAGS * SPAN).bit_length()
    column_block = min(D, 512)
    groups = D // column_block

    def convolve(pair):
        series, kernel = pair
        spectrum = jnp.fft.rfft(series, n=fft_len, axis=0) * jnp.fft.rfft(kernel, n=fft_len, axis=0)
        return jnp.fft.irfft(spectrum, n=fft_len, axis=0)[:extent]

    series = natural.reshape(TOKENS, groups, column_block).transpose(1, 0, 2)
    kernel = filter_taps.reshape(LAGS * SPAN, groups, column_block).transpose(1, 0, 2)
    full = lax.map(convolve, (series, kernel))
    full = full.transpose(1, 0, 2).reshape(extent, D).astype(jnp.float32)
    conv_cycle = full[:TOKENS].reshape(SPANS, SPAN, D)[span_order].reshape(TOKENS, D)
    mixed = (gate_act.astype(jnp.float32) * (conv_cycle + skip_gain[None, :] * signal.astype(jnp.float32))).astype(jnp.bfloat16)
    projected = jnp.dot(mixed, w_out, preferred_element_type=jnp.float32).astype(jnp.bfloat16)
    tail = full[TOKENS:].reshape(FUT_BLOCKS, SPAN, D)[decode_order].reshape(FUTURE, D)
    return projected, tail
```

```python
import math

import jax
import jax.numpy as jnp
from jax import lax
from jax.sharding import PartitionSpec as P

SPAN = 256

HIGH = lax.Precision.HIGH


def forward_table(length):
    half = length // 2
    rows_idx = lax.broadcasted_iota(jnp.int32, (length, length), 0)
    cols_idx = lax.broadcasted_iota(jnp.int32, (length, length), 1)
    frequency = rows_idx % half
    phase = (frequency * cols_idx % length).astype(jnp.float32) * (2.0 * math.pi / length)
    parity = (1 - 2 * (cols_idx % 2)).astype(jnp.float32)
    table = jnp.where(rows_idx < half, jnp.cos(phase), -jnp.sin(phase))
    return jnp.where(rows_idx == half, parity, table)


def inverse_table(length):
    half = length // 2
    rows_idx = lax.broadcasted_iota(jnp.int32, (half, length), 0)
    cols_idx = lax.broadcasted_iota(jnp.int32, (half, length), 1)
    frequency = cols_idx % half
    phase = (frequency * rows_idx % length).astype(jnp.float32) * (2.0 * math.pi / length)
    weight = jnp.where(frequency == 0, 1.0 / length, 2.0 / length)
    table = jnp.where(cols_idx < half, weight * jnp.cos(phase), -weight * jnp.sin(phase))
    parity = (1 - 2 * (rows_idx % 2)).astype(jnp.float32) / length
    return jnp.where(cols_idx == half, parity, table)


def spectral_product(left, right):
    half = left.shape[-2] // 2
    left_re, left_im = (left[..., :half, :], left[..., half:, :])
    right_re, right_im = (right[..., :half, :], right[..., half:, :])
    first = lax.broadcasted_iota(jnp.int32, left_re.shape, left_re.ndim - 2) == 0
    real_part = jnp.where(first, left_re * right_re, left_re * right_re - left_im * right_im)
    imag_part = jnp.where(first, left_im * right_im, left_re * right_im + left_im * right_re)
    return jnp.concatenate([real_part, imag_part], axis=-2)


def per_device(
    gate_act, key_act, value_act, filter_taps, skip_gain, w_out, span_order, decode_order
):
    width = gate_act.shape[1]
    length = 2 * SPAN
    cycle_size = lax.axis_size("ctx")
    position = lax.axis_index("ctx")
    count_spans = 2 * cycle_size
    count_lags = 3 * cycle_size
    forward = forward_table(length).astype(jnp.bfloat16)
    inverse = inverse_table(length)
    signal = (key_act.astype(jnp.float32) * value_act.astype(jnp.float32)).astype(jnp.bfloat16)

    all_taps = lax.all_gather(filter_taps.astype(jnp.bfloat16), "ctx", axis=0, tiled=True)
    blocks = all_taps.reshape(count_lags, SPAN, width)
    earlier = jnp.concatenate([jnp.zeros((1, SPAN, width), jnp.bfloat16), blocks[:-1]], axis=0)
    seg_spec = jnp.einsum(
        "kn,anc->akc", forward[:, :SPAN], blocks, preferred_element_type=jnp.float32
    ) + jnp.einsum(
        "kn,anc->akc", forward[:, SPAN + 1 :], earlier[:, 1:, :], preferred_element_type=jnp.float32
    )

    piece = lax.all_gather(signal, "ctx", axis=0, tiled=True)
    span_spec = jnp.einsum(
        "kn,anc->akc",
        forward[:, :SPAN],
        piece.reshape(count_spans, SPAN, width),
        preferred_element_type=jnp.float32,
    )

    my_spans = lax.dynamic_slice_in_dim(span_order, 2 * position, 2)
    my_future = count_spans + lax.dynamic_index_in_dim(decode_order, position, keepdims=False)
    targets = jnp.concatenate([my_spans, my_future[None]])
    lags = targets[:, None] - span_order[None, :]
    picked = jnp.take(seg_spec, jnp.maximum(lags, 0), axis=0)
    terms = spectral_product(picked, span_spec[None])
    totals = jnp.sum(jnp.where((lags >= 0)[:, :, None, None], terms, 0.0), axis=1)
    blocks_out = jnp.einsum(
        "nk,akc->anc", inverse, totals, precision=HIGH, preferred_element_type=jnp.float32
    )
    conv = blocks_out[:2].reshape(2 * SPAN, width)
    tail = blocks_out[2]
    mixed = (
        gate_act.astype(jnp.float32) * (conv + skip_gain[None, :] * signal.astype(jnp.float32))
    ).astype(jnp.bfloat16)
    summed = jnp.dot(
        lax.all_gather(mixed, "ch", axis=1, tiled=True), w_out, preferred_element_type=jnp.float32
    )
    projected = summed.astype(jnp.bfloat16)
    return (projected, tail)


def solution(mesh):
    in_specs = (
        P("ctx", "ch"),
        P("ctx", "ch"),
        P("ctx", "ch"),
        P("ctx", "ch"),
        P("ch"),
        P(None, "ch"),
        P(),
        P(),
    )
    out_specs = (P("ctx", "ch"), P("ctx", "ch"))
    return jax.shard_map(
        per_device, mesh=mesh, in_specs=in_specs, out_specs=out_specs, check_vma=False
    )
```

```python
import math

import jax
import jax.numpy as jnp
from jax import lax
from jax.experimental import pallas as pl
from jax.experimental.pallas import tpu as pltpu
from jax.sharding import Mesh, PartitionSpec as P

SPAN = 256

HIGH = lax.Precision.HIGH


def forward_table(length):
    half = length // 2
    rows_idx = lax.broadcasted_iota(jnp.int32, (length, length), 0)
    cols_idx = lax.broadcasted_iota(jnp.int32, (length, length), 1)
    frequency = rows_idx % half
    phase = (frequency * cols_idx % length).astype(jnp.float32) * (2.0 * math.pi / length)
    parity = (1 - 2 * (cols_idx % 2)).astype(jnp.float32)
    table = jnp.where(rows_idx < half, jnp.cos(phase), -jnp.sin(phase))
    return jnp.where(rows_idx == half, parity, table)


def inverse_table(length):
    half = length // 2
    rows_idx = lax.broadcasted_iota(jnp.int32, (half, length), 0)
    cols_idx = lax.broadcasted_iota(jnp.int32, (half, length), 1)
    frequency = cols_idx % half
    phase = (frequency * rows_idx % length).astype(jnp.float32) * (2.0 * math.pi / length)
    weight = jnp.where(frequency == 0, 1.0 / length, 2.0 / length)
    table = jnp.where(cols_idx < half, weight * jnp.cos(phase), -weight * jnp.sin(phase))
    parity = (1 - 2 * (rows_idx % 2)).astype(jnp.float32) / length
    return jnp.where(cols_idx == half, parity, table)


def spectral_product(left, right):
    half = left.shape[-2] // 2
    left_re, left_im = (left[..., :half, :], left[..., half:, :])
    right_re, right_im = (right[..., :half, :], right[..., half:, :])
    first = lax.broadcasted_iota(jnp.int32, left_re.shape, left_re.ndim - 2) == 0
    real_part = jnp.where(first, left_re * right_re, left_re * right_re - left_im * right_im)
    imag_part = jnp.where(first, left_im * right_im, left_re * right_im + left_im * right_re)
    return jnp.concatenate([real_part, imag_part], axis=-2)


def products(seg2d, span2d, lag_idx, lag_ok, n_targets, width, kt=32):
    half = seg2d.shape[0] // 2
    n_slots = span2d.shape[1] // width
    steps = half // kt

    def kernel(lag_ref, ok_ref, seg_re, seg_im, sp_re, sp_im, out_re, out_im):
        row = lax.broadcasted_iota(jnp.int32, (kt, width), 0)
        first = (pl.program_id(0) == 0) & (row == 0)
        for a in range(n_targets):
            acc_re = jnp.zeros((kt, width), jnp.float32)
            acc_im = jnp.zeros((kt, width), jnp.float32)
            for i in range(n_slots):
                lag = lag_ref[a * n_slots + i]
                w = ok_ref[a * n_slots + i].astype(jnp.float32)
                off = pl.multiple_of(lag * width, width)
                lr = seg_re[:, pl.ds(off, width)]
                li = seg_im[:, pl.ds(off, width)]
                rr = sp_re[:, i * width:(i + 1) * width]
                ri = sp_im[:, i * width:(i + 1) * width]
                cross = li * ri
                re = lr * rr - jnp.where(first, 0.0, cross)
                im = jnp.where(first, cross, lr * ri + li * rr)
                acc_re = acc_re + w * re
                acc_im = acc_im + w * im
            out_re[:, a * width:(a + 1) * width] = acc_re
            out_im[:, a * width:(a + 1) * width] = acc_im

    seg_cols = seg2d.shape[1]
    span_cols = span2d.shape[1]
    grid_spec = pltpu.PrefetchScalarGridSpec(
        num_scalar_prefetch=2,
        grid=(steps,),
        in_specs=[
            pl.BlockSpec((kt, seg_cols), lambda i, l, o: (i, 0)),
            pl.BlockSpec((kt, seg_cols), lambda i, l, o: (i + steps, 0)),
            pl.BlockSpec((kt, span_cols), lambda i, l, o: (i, 0)),
            pl.BlockSpec((kt, span_cols), lambda i, l, o: (i + steps, 0)),
        ],
        out_specs=[
            pl.BlockSpec((kt, n_targets * width), lambda i, l, o: (i, 0)),
            pl.BlockSpec((kt, n_targets * width), lambda i, l, o: (i, 0)),
        ],
    )
    out_shape = [jax.ShapeDtypeStruct((half, n_targets * width), jnp.float32)] * 2
    re, im = pl.pallas_call(kernel, grid_spec=grid_spec, out_shape=out_shape)(
        lag_idx, lag_ok, seg2d, seg2d, span2d, span2d)
    return jnp.concatenate([re, im], axis=0)


def gather_rows(x, axis):
    count = lax.axis_size(axis)
    position = lax.axis_index(axis)
    parts = [x] + [
        lax.ppermute(x, axis, [(i, (i + shift) % count) for i in range(count)])
        for shift in range(1, count)
    ]
    stacked = jnp.stack(parts)
    return jnp.take(stacked, (position - jnp.arange(count)) % count, axis=0)


def per_device(
    gate_act, key_act, value_act, filter_taps, skip_gain, w_out, span_order, decode_order
):
    width = gate_act.shape[1]
    length = 2 * SPAN
    cycle_size = lax.axis_size("ctx")
    position = lax.axis_index("ctx")
    count_spans = 2 * cycle_size
    count_lags = 3 * cycle_size
    forward = forward_table(length).astype(jnp.bfloat16)
    inverse = inverse_table(length)
    signal = (key_act.astype(jnp.float32) * value_act.astype(jnp.float32)).astype(jnp.bfloat16)

    gathered = gather_rows(
        jnp.concatenate([filter_taps.astype(jnp.bfloat16), signal], axis=0), "ctx"
    )
    tap_rows = filter_taps.shape[0]
    blocks = gathered[:, :tap_rows].reshape(count_lags, SPAN, width)
    piece = gathered[:, tap_rows:].reshape(count_spans, SPAN, width)

    earlier = jnp.concatenate([jnp.zeros((1, SPAN, width), jnp.bfloat16), blocks[:-1]], axis=0)
    segments = jnp.concatenate(
        [blocks, jnp.zeros((count_lags, 1, width), jnp.bfloat16), earlier[:, 1:, :]], axis=1
    )
    seg_spec = jnp.einsum(
        "kn,anc->kac", forward, segments, preferred_element_type=jnp.float32
    ).reshape(length, count_lags * width)
    span_spec = jnp.einsum(
        "kn,anc->kac", forward[:, :SPAN], piece, preferred_element_type=jnp.float32
    ).reshape(length, count_spans * width)

    my_spans = lax.dynamic_slice_in_dim(span_order, 2 * position, 2)
    my_future = count_spans + lax.dynamic_index_in_dim(decode_order, position, keepdims=False)
    targets = jnp.concatenate([my_spans, my_future[None]])
    lags = targets[:, None] - span_order[None, :]
    totals = products(
        seg_spec,
        span_spec,
        jnp.maximum(lags, 0).reshape(-1),
        (lags >= 0).astype(jnp.int32).reshape(-1),
        3,
        width,
    )
    blocks_out = jnp.dot(inverse, totals, precision=HIGH, preferred_element_type=jnp.float32)
    conv = jnp.concatenate([blocks_out[:, :width], blocks_out[:, width : 2 * width]], axis=0)
    tail = blocks_out[:, 2 * width :]
    mixed = (
        gate_act.astype(jnp.float32) * (conv + skip_gain[None, :] * signal.astype(jnp.float32))
    ).astype(jnp.bfloat16)

    pair = gather_rows(mixed, "xlo")
    pair = jnp.moveaxis(pair, 0, 1).reshape(mixed.shape[0], -1)
    ring = lax.all_gather(pair, "z", axis=1, tiled=True)
    full = gather_rows(ring, "core")
    full = jnp.moveaxis(full, 0, 1).reshape(mixed.shape[0], -1)
    count_z = lax.axis_size("z")
    count_xlo = lax.axis_size("xlo")
    count_core = lax.axis_size("core")
    w_perm = (
        w_out.reshape(count_z, count_xlo, count_core, width, w_out.shape[1])
        .transpose(2, 0, 1, 3, 4)
        .reshape(w_out.shape)
    )
    summed = jnp.dot(full, w_perm, preferred_element_type=jnp.float32)
    projected = summed.astype(jnp.bfloat16)
    return (projected, tail)


def solution(mesh):
    ch = mesh.shape["ch"]
    fine = Mesh(
        mesh.devices.reshape(mesh.shape["ctx"], ch // 4, 2, 2), ("ctx", "z", "xlo", "core")
    )
    chans = ("z", "xlo", "core")
    in_specs = (
        P("ctx", chans),
        P("ctx", chans),
        P("ctx", chans),
        P("ctx", chans),
        P(chans),
        P(None, chans),
        P(),
        P(),
    )
    out_specs = (P("ctx", chans), P("ctx", chans))
    return jax.shard_map(
        per_device, mesh=fine, in_specs=in_specs, out_specs=out_specs, check_vma=False
    )
```

```python
import math

import jax
import jax.numpy as jnp
from jax import lax
from jax.experimental import pallas as pl
from jax.experimental.pallas import tpu as pltpu
from jax.sharding import Mesh, PartitionSpec as P

SPAN = 256

HIGH = lax.Precision.HIGH


def forward_table(length):
    half = length // 2
    rows_idx = lax.broadcasted_iota(jnp.int32, (length, length), 0)
    cols_idx = lax.broadcasted_iota(jnp.int32, (length, length), 1)
    frequency = rows_idx % half
    phase = (frequency * cols_idx % length).astype(jnp.float32) * (2.0 * math.pi / length)
    parity = (1 - 2 * (cols_idx % 2)).astype(jnp.float32)
    table = jnp.where(rows_idx < half, jnp.cos(phase), -jnp.sin(phase))
    return jnp.where(rows_idx == half, parity, table)


def inverse_table(length):
    half = length // 2
    rows_idx = lax.broadcasted_iota(jnp.int32, (half, length), 0)
    cols_idx = lax.broadcasted_iota(jnp.int32, (half, length), 1)
    frequency = cols_idx % half
    phase = (frequency * rows_idx % length).astype(jnp.float32) * (2.0 * math.pi / length)
    weight = jnp.where(frequency == 0, 1.0 / length, 2.0 / length)
    table = jnp.where(cols_idx < half, weight * jnp.cos(phase), -weight * jnp.sin(phase))
    parity = (1 - 2 * (rows_idx % 2)).astype(jnp.float32) / length
    return jnp.where(cols_idx == half, parity, table)


def spectral_product(left, right):
    half = left.shape[-2] // 2
    left_re, left_im = (left[..., :half, :], left[..., half:, :])
    right_re, right_im = (right[..., :half, :], right[..., half:, :])
    first = lax.broadcasted_iota(jnp.int32, left_re.shape, left_re.ndim - 2) == 0
    real_part = jnp.where(first, left_re * right_re, left_re * right_re - left_im * right_im)
    imag_part = jnp.where(first, left_im * right_im, left_re * right_im + left_im * right_re)
    return jnp.concatenate([real_part, imag_part], axis=-2)


def products(seg2d, span2d, lag_idx, lag_ok, n_targets, width, kt=32):
    half = seg2d.shape[0] // 2
    n_slots = span2d.shape[1] // width
    steps = half // kt

    def kernel(lag_ref, ok_ref, seg_re, seg_im, sp_re, sp_im, out_re, out_im):
        row = lax.broadcasted_iota(jnp.int32, (kt, width), 0)
        first = (pl.program_id(0) == 0) & (row == 0)
        for a in range(n_targets):
            acc_re = jnp.zeros((kt, width), jnp.float32)
            acc_im = jnp.zeros((kt, width), jnp.float32)
            for i in range(n_slots):
                lag = lag_ref[a * n_slots + i]
                w = ok_ref[a * n_slots + i].astype(jnp.float32)
                off = pl.multiple_of(lag * width, width)
                lr = seg_re[:, pl.ds(off, width)]
                li = seg_im[:, pl.ds(off, width)]
                rr = sp_re[:, i * width:(i + 1) * width]
                ri = sp_im[:, i * width:(i + 1) * width]
                cross = li * ri
                re = lr * rr - jnp.where(first, 0.0, cross)
                im = jnp.where(first, cross, lr * ri + li * rr)
                acc_re = acc_re + w * re
                acc_im = acc_im + w * im
            out_re[:, a * width:(a + 1) * width] = acc_re
            out_im[:, a * width:(a + 1) * width] = acc_im

    seg_cols = seg2d.shape[1]
    span_cols = span2d.shape[1]
    grid_spec = pltpu.PrefetchScalarGridSpec(
        num_scalar_prefetch=2,
        grid=(steps,),
        in_specs=[
            pl.BlockSpec((kt, seg_cols), lambda i, l, o: (i, 0)),
            pl.BlockSpec((kt, seg_cols), lambda i, l, o: (i + steps, 0)),
            pl.BlockSpec((kt, span_cols), lambda i, l, o: (i, 0)),
            pl.BlockSpec((kt, span_cols), lambda i, l, o: (i + steps, 0)),
        ],
        out_specs=[
            pl.BlockSpec((kt, n_targets * width), lambda i, l, o: (i, 0)),
            pl.BlockSpec((kt, n_targets * width), lambda i, l, o: (i, 0)),
        ],
    )
    out_shape = [jax.ShapeDtypeStruct((half, n_targets * width), jnp.float32)] * 2
    re, im = pl.pallas_call(kernel, grid_spec=grid_spec, out_shape=out_shape)(
        lag_idx, lag_ok, seg2d, seg2d, span2d, span2d)
    return jnp.concatenate([re, im], axis=0)


def swap(x, axis):
    count = lax.axis_size(axis)
    return lax.ppermute(x, axis, [(i, (i + 1) % count) for i in range(count)])


def per_device(
    gate_act, key_act, value_act, filter_taps, skip_gain, w_out, span_order, decode_order
):
    width = gate_act.shape[1]
    length = 2 * SPAN
    cycle_size = lax.axis_size("ctx")
    position = lax.axis_index("ctx")
    count_spans = 2 * cycle_size
    count_lags = 3 * cycle_size
    forward = forward_table(length).astype(jnp.bfloat16)
    inverse = inverse_table(length)
    signal = (key_act.astype(jnp.float32) * value_act.astype(jnp.float32)).astype(jnp.bfloat16)

    own = jnp.concatenate([filter_taps.astype(jnp.bfloat16), signal], axis=0)
    parts = [own] + [
        lax.ppermute(own, "ctx", [(i, (i + shift) % cycle_size) for i in range(cycle_size)])
        for shift in range(1, cycle_size)
    ]
    stacked = jnp.stack(parts)
    tap_rows = filter_taps.shape[0]
    per_lag = tap_rows // SPAN
    per_span = signal.shape[0] // SPAN
    blocks = stacked[:, :tap_rows].reshape(cycle_size, per_lag, SPAN, width)
    piece = stacked[:, tap_rows:].reshape(cycle_size, per_span, SPAN, width)

    previous = jnp.roll(blocks[:, per_lag - 1 :], -1, axis=0)
    first_part = (jnp.arange(cycle_size) == position)[:, None, None, None]
    previous = jnp.where(first_part, jnp.zeros_like(previous), previous)
    earlier = jnp.concatenate([previous, blocks[:, : per_lag - 1]], axis=1)
    seg_time = jnp.concatenate(
        [
            blocks.transpose(2, 0, 1, 3),
            jnp.zeros((1, cycle_size, per_lag, width), jnp.bfloat16),
            earlier[:, :, 1:].transpose(2, 0, 1, 3),
        ],
        axis=0,
    ).reshape(length, count_lags * width)
    seg_spec = jnp.dot(forward, seg_time, preferred_element_type=jnp.float32)
    span_time = piece.transpose(2, 0, 1, 3).reshape(SPAN, count_spans * width)
    span_spec = jnp.dot(forward[:, :SPAN], span_time, preferred_element_type=jnp.float32)

    held = jnp.arange(count_spans)
    global_slot = per_span * ((position - held // per_span) % cycle_size) + held % per_span
    held_spans = span_order[global_slot]
    my_spans = lax.dynamic_slice_in_dim(span_order, per_span * position, per_span)
    my_future = count_spans + lax.dynamic_index_in_dim(decode_order, position, keepdims=False)
    targets = jnp.concatenate([my_spans, my_future[None]])
    lags = targets[:, None] - held_spans[None, :]
    valid = lags >= 0
    lag = jnp.maximum(lags, 0)
    column = per_lag * ((position - lag // per_lag) % cycle_size) + lag % per_lag
    totals = products(
        seg_spec,
        span_spec,
        column.reshape(-1),
        valid.astype(jnp.int32).reshape(-1),
        targets.shape[0],
        width,
    )
    blocks_out = jnp.dot(inverse, totals, precision=HIGH, preferred_element_type=jnp.float32)
    conv = jnp.concatenate([blocks_out[:, :width], blocks_out[:, width : 2 * width]], axis=0)
    tail = blocks_out[:, 2 * width :]
    mixed = (
        gate_act.astype(jnp.float32) * (conv + skip_gain[None, :] * signal.astype(jnp.float32))
    ).astype(jnp.bfloat16)

    count_z = lax.axis_size("z")
    xlo = lax.axis_index("xlo")
    core = lax.axis_index("core")
    w5 = w_out.reshape(count_z, 2, 2, width, w_out.shape[1])
    w5 = jnp.where(xlo == 0, w5, jnp.flip(w5, axis=1))
    rows = count_z * 2 * width
    w_own = lax.dynamic_index_in_dim(w5, core, axis=2, keepdims=False).reshape(rows, -1)
    w_other = lax.dynamic_index_in_dim(w5, 1 - core, axis=2, keepdims=False).reshape(rows, -1)

    pair = jnp.concatenate([mixed, swap(mixed, "xlo")], axis=1)
    ring = lax.all_gather(pair, "z", axis=1, tiled=True)
    summed = jnp.dot(ring, w_own, preferred_element_type=jnp.float32) + jnp.dot(
        swap(ring, "core"), w_other, preferred_element_type=jnp.float32
    )
    projected = summed.astype(jnp.bfloat16)
    return (projected, tail)


def solution(mesh):
    ch = mesh.shape["ch"]
    fine = Mesh(
        mesh.devices.reshape(mesh.shape["ctx"], ch // 4, 2, 2), ("ctx", "z", "xlo", "core")
    )
    chans = ("z", "xlo", "core")
    in_specs = (
        P("ctx", chans),
        P("ctx", chans),
        P("ctx", chans),
        P("ctx", chans),
        P(chans),
        P(None, chans),
        P(),
        P(),
    )
    out_specs = (P("ctx", chans), P("ctx", chans))
    return jax.shard_map(
        per_device, mesh=fine, in_specs=in_specs, out_specs=out_specs, check_vma=False
    )
```

```python
import math

import jax
import jax.numpy as jnp
from jax import lax
from jax.experimental import pallas as pl
from jax.experimental.pallas import tpu as pltpu
from jax.sharding import Mesh, PartitionSpec as P


SPAN = 256


HIGH = lax.Precision.HIGH


def forward_table(length):
    half = length // 2
    rows_idx = lax.broadcasted_iota(jnp.int32, (length, length), 0)
    cols_idx = lax.broadcasted_iota(jnp.int32, (length, length), 1)
    frequency = rows_idx % half
    phase = (frequency * cols_idx % length).astype(jnp.float32) * (2.0 * math.pi / length)
    parity = (1 - 2 * (cols_idx % 2)).astype(jnp.float32)
    table = jnp.where(rows_idx < half, jnp.cos(phase), -jnp.sin(phase))
    return jnp.where(rows_idx == half, parity, table)


def inverse_table(length):
    half = length // 2
    rows_idx = lax.broadcasted_iota(jnp.int32, (half, length), 0)
    cols_idx = lax.broadcasted_iota(jnp.int32, (half, length), 1)
    frequency = cols_idx % half
    phase = (frequency * rows_idx % length).astype(jnp.float32) * (2.0 * math.pi / length)
    weight = jnp.where(frequency == 0, 1.0 / length, 2.0 / length)
    table = jnp.where(cols_idx < half, weight * jnp.cos(phase), -weight * jnp.sin(phase))
    parity = (1 - 2 * (rows_idx % 2)).astype(jnp.float32) / length
    return jnp.where(cols_idx == half, parity, table)


def products(seg2d, span2d, lag_idx, lag_ok, n_targets, width, kt=32):
    half = seg2d.shape[0] // 2
    n_slots = span2d.shape[1] // width
    steps = half // kt

    def kernel(lag_ref, ok_ref, seg_re, seg_im, sp_re, sp_im, out_re, out_im):
        row = lax.broadcasted_iota(jnp.int32, (kt, width), 0)
        first = (pl.program_id(0) == 0) & (row == 0)
        for a in range(n_targets):

            def step(i, acc, a=a):
                acc_re, acc_im = acc
                lag = lag_ref[a * n_slots + i]
                w = ok_ref[a * n_slots + i].astype(jnp.float32)
                off = pl.multiple_of(lag * width, width)
                own = pl.multiple_of(i * width, width)
                lr = seg_re[:, pl.ds(off, width)]
                li = seg_im[:, pl.ds(off, width)]
                rr = sp_re[:, pl.ds(own, width)]
                ri = sp_im[:, pl.ds(own, width)]
                cross = li * ri
                re = lr * rr - jnp.where(first, 0.0, cross)
                im = jnp.where(first, cross, lr * ri + li * rr)
                return (acc_re + w * re, acc_im + w * im)

            zero = jnp.zeros((kt, width), jnp.float32)
            acc_re, acc_im = lax.fori_loop(0, n_slots, step, (zero, zero), unroll=4)
            out_re[:, a * width:(a + 1) * width] = acc_re
            out_im[:, a * width:(a + 1) * width] = acc_im

    seg_cols = seg2d.shape[1]
    span_cols = span2d.shape[1]
    grid_spec = pltpu.PrefetchScalarGridSpec(
        num_scalar_prefetch=2,
        grid=(steps,),
        in_specs=[
            pl.BlockSpec((kt, seg_cols), lambda i, l, o: (i, 0)),
            pl.BlockSpec((kt, seg_cols), lambda i, l, o: (i + steps, 0)),
            pl.BlockSpec((kt, span_cols), lambda i, l, o: (i, 0)),
            pl.BlockSpec((kt, span_cols), lambda i, l, o: (i + steps, 0)),
        ],
        out_specs=[
            pl.BlockSpec((kt, n_targets * width), lambda i, l, o: (i, 0)),
            pl.BlockSpec((kt, n_targets * width), lambda i, l, o: (i, 0)),
        ],
    )
    out_shape = [jax.ShapeDtypeStruct((half, n_targets * width), jnp.float32)] * 2
    re, im = pl.pallas_call(kernel, grid_spec=grid_spec, out_shape=out_shape)(
        lag_idx, lag_ok, seg2d, seg2d, span2d, span2d)
    return jnp.concatenate([re, im], axis=0)


def swap(x, axis):
    count = lax.axis_size(axis)
    return lax.ppermute(x, axis, [(i, (i + 1) % count) for i in range(count)])


def channel_part(
    gate_act, key_act, value_act, filter_taps, skip_gain, w_rows, span_order, decode_order, after
):
    width = gate_act.shape[1]
    length = 2 * SPAN
    cycle_size = lax.axis_size("ctx")
    position = lax.axis_index("ctx")
    count_spans = 2 * cycle_size
    count_lags = 3 * cycle_size
    forward = forward_table(length).astype(jnp.bfloat16)
    inverse = inverse_table(length)
    signal = (key_act.astype(jnp.float32) * value_act.astype(jnp.float32)).astype(jnp.bfloat16)

    own = jnp.concatenate([filter_taps.astype(jnp.bfloat16), signal], axis=0)
    forward, inverse, own = lax.optimization_barrier((forward, inverse, own))
    parts = [own] + [
        lax.ppermute(own, "ctx", [(i, (i + shift) % cycle_size) for i in range(cycle_size)])
        for shift in range(1, cycle_size)
    ]
    stacked = jnp.stack(parts)
    if after is not None:
        stacked, _ = lax.optimization_barrier((stacked, after))
    tap_rows = filter_taps.shape[0]
    per_lag = tap_rows // SPAN
    per_span = signal.shape[0] // SPAN
    blocks = stacked[:, :tap_rows].reshape(cycle_size, per_lag, SPAN, width)
    piece = stacked[:, tap_rows:].reshape(cycle_size, per_span, SPAN, width)

    previous = jnp.roll(blocks[:, per_lag - 1 :], -1, axis=0)
    first_part = (jnp.arange(cycle_size) == position)[:, None, None, None]
    previous = jnp.where(first_part, jnp.zeros_like(previous), previous)
    earlier = jnp.concatenate([previous, blocks[:, : per_lag - 1]], axis=1)
    seg_time = jnp.concatenate(
        [
            blocks.transpose(2, 0, 1, 3),
            jnp.zeros((1, cycle_size, per_lag, width), jnp.bfloat16),
            earlier[:, :, 1:].transpose(2, 0, 1, 3),
        ],
        axis=0,
    ).reshape(length, count_lags * width)
    seg_spec = jnp.dot(forward, seg_time, preferred_element_type=jnp.float32)
    span_time = piece.transpose(2, 0, 1, 3).reshape(SPAN, count_spans * width)
    span_spec = jnp.dot(forward[:, :SPAN], span_time, preferred_element_type=jnp.float32)

    held = jnp.arange(count_spans)
    global_slot = per_span * ((position - held // per_span) % cycle_size) + held % per_span
    held_spans = span_order[global_slot]
    my_spans = lax.dynamic_slice_in_dim(span_order, per_span * position, per_span)
    my_future = count_spans + lax.dynamic_index_in_dim(decode_order, position, keepdims=False)
    targets = jnp.concatenate([my_spans, my_future[None]])
    lags = targets[:, None] - held_spans[None, :]
    valid = lags >= 0
    lag = jnp.maximum(lags, 0)
    column = per_lag * ((position - lag // per_lag) % cycle_size) + lag % per_lag
    totals = products(
        seg_spec,
        span_spec,
        column.reshape(-1),
        valid.astype(jnp.int32).reshape(-1),
        targets.shape[0],
        width,
    )
    blocks_out = jnp.dot(inverse, totals, precision=HIGH, preferred_element_type=jnp.float32)
    conv = jnp.concatenate([blocks_out[:, :width], blocks_out[:, width : 2 * width]], axis=0)
    tail = blocks_out[:, 2 * width :]
    mixed = (
        gate_act.astype(jnp.float32) * (conv + skip_gain[None, :] * signal.astype(jnp.float32))
    ).astype(jnp.bfloat16)

    xlo = lax.axis_index("xlo")
    other = swap(mixed, "xlo")
    pair = jnp.where(
        xlo == 0,
        jnp.concatenate([mixed, other], axis=1),
        jnp.concatenate([other, mixed], axis=1),
    )
    ring = lax.all_gather(pair, "z", axis=1, tiled=True)
    w_own, w_other = w_rows
    summed = jnp.dot(ring, w_own, preferred_element_type=jnp.float32) + jnp.dot(
        swap(ring, "core"), w_other, preferred_element_type=jnp.float32
    )
    return summed, tail, mixed


def halves_of(
    gate_act, key_act, value_act, filter_taps, skip_gain, w_out, span_order, decode_order
):
    width = gate_act.shape[1]
    count_z = lax.axis_size("z")
    core = lax.axis_index("core")
    w5 = w_out.reshape(count_z, 2, 2, width, w_out.shape[1])
    w_own_all = lax.dynamic_index_in_dim(w5, core, axis=2, keepdims=False)
    w_other_all = lax.dynamic_index_in_dim(w5, 1 - core, axis=2, keepdims=False)
    halves = 2
    part_width = width // halves
    total = None
    previous = None
    tails = []
    for half in range(halves):
        cols = slice(half * part_width, (half + 1) * part_width)
        rows = count_z * 2 * part_width
        w_rows = (
            w_own_all[:, :, cols].reshape(rows, -1),
            w_other_all[:, :, cols].reshape(rows, -1),
        )
        summed, tail, previous = channel_part(
            gate_act[:, cols],
            key_act[:, cols],
            value_act[:, cols],
            filter_taps[:, cols],
            skip_gain[cols],
            w_rows,
            span_order,
            decode_order,
            previous,
        )
        total = summed if total is None else total + summed
        tails.append(tail)
    projected = total.astype(jnp.bfloat16)
    return (projected, jnp.concatenate(tails, axis=1))


def solution(mesh):
    ch = mesh.shape["ch"]
    fine = Mesh(
        mesh.devices.reshape(mesh.shape["ctx"], ch // 4, 2, 2), ("ctx", "z", "xlo", "core")
    )
    chans = ("z", "xlo", "core")
    in_specs = (
        P("ctx", chans),
        P("ctx", chans),
        P("ctx", chans),
        P("ctx", chans),
        P(chans),
        P(None, chans),
        P(),
        P(),
    )
    out_specs = (P("ctx", chans), P("ctx", chans))
    return jax.shard_map(
        halves_of, mesh=fine, in_specs=in_specs, out_specs=out_specs, check_vma=False
    )
```

```python
import math

import jax
import jax.numpy as jnp
from jax import lax
from jax.experimental import pallas as pl
from jax.experimental.pallas import tpu as pltpu
from jax.sharding import Mesh, PartitionSpec as P


SPAN = 256


HIGH = lax.Precision.HIGH


def forward_table(length):
    half = length // 2
    rows_idx = lax.broadcasted_iota(jnp.int32, (length, length), 0)
    cols_idx = lax.broadcasted_iota(jnp.int32, (length, length), 1)
    frequency = rows_idx % half
    phase = (frequency * cols_idx % length).astype(jnp.float32) * (2.0 * math.pi / length)
    parity = (1 - 2 * (cols_idx % 2)).astype(jnp.float32)
    table = jnp.where(rows_idx < half, jnp.cos(phase), -jnp.sin(phase))
    return jnp.where(rows_idx == half, parity, table)


def inverse_table(length):
    half = length // 2
    rows_idx = lax.broadcasted_iota(jnp.int32, (half, length), 0)
    cols_idx = lax.broadcasted_iota(jnp.int32, (half, length), 1)
    frequency = cols_idx % half
    phase = (frequency * rows_idx % length).astype(jnp.float32) * (2.0 * math.pi / length)
    weight = jnp.where(frequency == 0, 1.0 / length, 2.0 / length)
    table = jnp.where(cols_idx < half, weight * jnp.cos(phase), -weight * jnp.sin(phase))
    parity = (1 - 2 * (rows_idx % 2)).astype(jnp.float32) / length
    return jnp.where(cols_idx == half, parity, table)


def products(seg2d, span2d, lag_idx, lag_ok, n_targets, width, kt=32):
    half = seg2d.shape[0] // 2
    n_slots = span2d.shape[1] // width
    steps = half // kt

    def kernel(lag_ref, ok_ref, seg_re, seg_im, sp_re, sp_im, out_re, out_im):
        row = lax.broadcasted_iota(jnp.int32, (kt, width), 0)
        first = (pl.program_id(0) == 0) & (row == 0)
        for a in range(n_targets):

            def step(i, acc, a=a):
                acc_re, acc_im = acc
                lag = lag_ref[a * n_slots + i]
                w = ok_ref[a * n_slots + i].astype(jnp.float32)
                off = pl.multiple_of(lag * width, width)
                own = pl.multiple_of(i * width, width)
                lr = seg_re[:, pl.ds(off, width)]
                li = seg_im[:, pl.ds(off, width)]
                rr = sp_re[:, pl.ds(own, width)]
                ri = sp_im[:, pl.ds(own, width)]
                cross = li * ri
                re = lr * rr - jnp.where(first, 0.0, cross)
                im = jnp.where(first, cross, lr * ri + li * rr)
                return (acc_re + w * re, acc_im + w * im)

            zero = jnp.zeros((kt, width), jnp.float32)
            acc_re, acc_im = lax.fori_loop(0, n_slots, step, (zero, zero), unroll=4)
            out_re[:, a * width:(a + 1) * width] = acc_re
            out_im[:, a * width:(a + 1) * width] = acc_im

    seg_cols = seg2d.shape[1]
    span_cols = span2d.shape[1]
    grid_spec = pltpu.PrefetchScalarGridSpec(
        num_scalar_prefetch=2,
        grid=(steps,),
        in_specs=[
            pl.BlockSpec((kt, seg_cols), lambda i, l, o: (i, 0)),
            pl.BlockSpec((kt, seg_cols), lambda i, l, o: (i + steps, 0)),
            pl.BlockSpec((kt, span_cols), lambda i, l, o: (i, 0)),
            pl.BlockSpec((kt, span_cols), lambda i, l, o: (i + steps, 0)),
        ],
        out_specs=[
            pl.BlockSpec((kt, n_targets * width), lambda i, l, o: (i, 0)),
            pl.BlockSpec((kt, n_targets * width), lambda i, l, o: (i, 0)),
        ],
    )
    out_shape = [jax.ShapeDtypeStruct((half, n_targets * width), jnp.float32)] * 2
    re, im = pl.pallas_call(kernel, grid_spec=grid_spec, out_shape=out_shape)(
        lag_idx, lag_ok, seg2d, seg2d, span2d, span2d)
    return jnp.concatenate([re, im], axis=0)


def swap(x, axis):
    count = lax.axis_size(axis)
    return lax.ppermute(x, axis, [(i, (i + 1) % count) for i in range(count)])


def channel_part(
    gate_act, key_act, value_act, filter_taps, skip_gain, span_order, decode_order, before, after
):
    width = gate_act.shape[1]
    length = 2 * SPAN
    cycle_size = lax.axis_size("ctx")
    position = lax.axis_index("ctx")
    count_spans = 2 * cycle_size
    count_lags = 3 * cycle_size
    forward = forward_table(length).astype(jnp.bfloat16)
    inverse = inverse_table(length)
    signal = (key_act.astype(jnp.float32) * value_act.astype(jnp.float32)).astype(jnp.bfloat16)

    own = jnp.concatenate([filter_taps.astype(jnp.bfloat16), signal], axis=0)
    forward, inverse, own = lax.optimization_barrier((forward, inverse, own))
    if before is not None:
        own, _ = lax.optimization_barrier((own, before))
    parts = [own] + [
        lax.ppermute(own, "ctx", [(i, (i + shift) % cycle_size) for i in range(cycle_size)])
        for shift in range(1, cycle_size)
    ]
    stacked = jnp.stack(parts)
    if after is not None:
        stacked, _ = lax.optimization_barrier((stacked, after))
    tap_rows = filter_taps.shape[0]
    per_lag = tap_rows // SPAN
    per_span = signal.shape[0] // SPAN
    blocks = stacked[:, :tap_rows].reshape(cycle_size, per_lag, SPAN, width)
    piece = stacked[:, tap_rows:].reshape(cycle_size, per_span, SPAN, width)

    previous = jnp.roll(blocks[:, per_lag - 1 :], -1, axis=0)
    first_part = (jnp.arange(cycle_size) == position)[:, None, None, None]
    previous = jnp.where(first_part, jnp.zeros_like(previous), previous)
    earlier = jnp.concatenate([previous, blocks[:, : per_lag - 1]], axis=1)
    seg_time = jnp.concatenate(
        [
            blocks.transpose(2, 0, 1, 3),
            jnp.zeros((1, cycle_size, per_lag, width), jnp.bfloat16),
            earlier[:, :, 1:].transpose(2, 0, 1, 3),
        ],
        axis=0,
    ).reshape(length, count_lags * width)
    seg_spec = jnp.dot(forward, seg_time, preferred_element_type=jnp.float32)
    span_time = piece.transpose(2, 0, 1, 3).reshape(SPAN, count_spans * width)
    span_spec = jnp.dot(forward[:, :SPAN], span_time, preferred_element_type=jnp.float32)

    held = jnp.arange(count_spans)
    global_slot = per_span * ((position - held // per_span) % cycle_size) + held % per_span
    held_spans = span_order[global_slot]
    my_spans = lax.dynamic_slice_in_dim(span_order, per_span * position, per_span)
    my_future = count_spans + lax.dynamic_index_in_dim(decode_order, position, keepdims=False)
    targets = jnp.concatenate([my_spans, my_future[None]])
    lags = targets[:, None] - held_spans[None, :]
    valid = lags >= 0
    lag = jnp.maximum(lags, 0)
    column = per_lag * ((position - lag // per_lag) % cycle_size) + lag % per_lag
    totals = products(
        seg_spec,
        span_spec,
        column.reshape(-1),
        valid.astype(jnp.int32).reshape(-1),
        targets.shape[0],
        width,
    )
    blocks_out = jnp.dot(inverse, totals, precision=HIGH, preferred_element_type=jnp.float32)
    conv = jnp.concatenate([blocks_out[:, :width], blocks_out[:, width : 2 * width]], axis=0)
    tail = blocks_out[:, 2 * width :]
    mixed = (
        gate_act.astype(jnp.float32) * (conv + skip_gain[None, :] * signal.astype(jnp.float32))
    ).astype(jnp.bfloat16)

    return tail, mixed, stacked


def halves_of(
    gate_act, key_act, value_act, filter_taps, skip_gain, w_out, span_order, decode_order
):
    width = gate_act.shape[1]
    count_z = lax.axis_size("z")
    core = lax.axis_index("core")
    xlo = lax.axis_index("xlo")
    w5 = w_out.reshape(count_z, 2, 2, width, w_out.shape[1])
    rows = count_z * 2 * width
    w_own = lax.dynamic_index_in_dim(w5, core, axis=2, keepdims=False).reshape(rows, -1)
    w_other = lax.dynamic_index_in_dim(w5, 1 - core, axis=2, keepdims=False).reshape(rows, -1)
    halves = 2
    part_width = width // halves
    received = None
    previous = None
    tails = []
    mixes = []
    for half in range(halves):
        cols = slice(half * part_width, (half + 1) * part_width)
        tail, previous, received = channel_part(
            gate_act[:, cols],
            key_act[:, cols],
            value_act[:, cols],
            filter_taps[:, cols],
            skip_gain[cols],
            span_order,
            decode_order,
            received,
            previous,
        )
        tails.append(tail)
        mixes.append(previous)
    mixed = jnp.concatenate(mixes, axis=1)

    other = swap(mixed, "xlo")
    pair = jnp.where(
        xlo == 0,
        jnp.concatenate([mixed, other], axis=1),
        jnp.concatenate([other, mixed], axis=1),
    )
    ring = lax.all_gather(pair, "z", axis=1, tiled=True)
    summed = jnp.dot(ring, w_own, preferred_element_type=jnp.float32) + jnp.dot(
        swap(ring, "core"), w_other, preferred_element_type=jnp.float32
    )
    projected = summed.astype(jnp.bfloat16)
    return (projected, jnp.concatenate(tails, axis=1))


def solution(mesh):
    ch = mesh.shape["ch"]
    fine = Mesh(
        mesh.devices.reshape(mesh.shape["ctx"], ch // 4, 2, 2), ("ctx", "z", "xlo", "core")
    )
    chans = ("z", "xlo", "core")
    in_specs = (
        P("ctx", chans),
        P("ctx", chans),
        P("ctx", chans),
        P("ctx", chans),
        P(chans),
        P(None, chans),
        P(),
        P(),
    )
    out_specs = (P("ctx", chans), P("ctx", chans))
    return jax.shard_map(
        halves_of, mesh=fine, in_specs=in_specs, out_specs=out_specs, check_vma=False
    )
```

```python
import math

import jax
import jax.numpy as jnp
from jax import lax
from jax.experimental import pallas as pl
from jax.experimental.pallas import tpu as pltpu
from jax.sharding import Mesh, PartitionSpec as P


SPAN = 256

HIGH = lax.Precision.HIGH


def forward_table(length):
    half = length // 2
    rows_idx = lax.broadcasted_iota(jnp.int32, (length, length), 0)
    cols_idx = lax.broadcasted_iota(jnp.int32, (length, length), 1)
    frequency = rows_idx % half
    phase = (frequency * cols_idx % length).astype(jnp.float32) * (2.0 * math.pi / length)
    parity = (1 - 2 * (cols_idx % 2)).astype(jnp.float32)
    table = jnp.where(rows_idx < half, jnp.cos(phase), -jnp.sin(phase))
    return jnp.where(rows_idx == half, parity, table)


def inverse_table(length):
    half = length // 2
    rows_idx = lax.broadcasted_iota(jnp.int32, (half, length), 0)
    cols_idx = lax.broadcasted_iota(jnp.int32, (half, length), 1)
    frequency = cols_idx % half
    phase = (frequency * rows_idx % length).astype(jnp.float32) * (2.0 * math.pi / length)
    weight = jnp.where(frequency == 0, 1.0 / length, 2.0 / length)
    table = jnp.where(cols_idx < half, weight * jnp.cos(phase), -weight * jnp.sin(phase))
    parity = (1 - 2 * (rows_idx % 2)).astype(jnp.float32) / length
    return jnp.where(cols_idx == half, parity, table)


def products(seg2d, span2d, lag_idx, lag_ok, n_targets, width, kt=32):
    half = seg2d.shape[0] // 2
    n_slots = span2d.shape[1] // width
    steps = half // kt

    def kernel(lag_ref, ok_ref, seg_re, seg_im, sp_re, sp_im, out_re, out_im):
        out_re[...] = jnp.zeros_like(out_re)
        out_im[...] = jnp.zeros_like(out_im)

        def operands(a, i, rows):
            off = pl.multiple_of(lag_ref[a * n_slots + i] * width, width)
            own = pl.multiple_of(i * width, width)
            return (
                seg_re[rows, pl.ds(off, width)],
                seg_im[rows, pl.ds(off, width)],
                sp_re[rows, pl.ds(own, width)],
                sp_im[rows, pl.ds(own, width)],
            )

        for a in range(n_targets):
            cols = slice(a * width, (a + 1) * width)

            def step(i, carry, a=a, cols=cols):
                @pl.when(ok_ref[a * n_slots + i] > 0)
                def _():
                    lr, li, rr, ri = operands(a, i, slice(None))
                    out_re[:, cols] += lr * rr - li * ri
                    out_im[:, cols] += lr * ri + li * rr

                return carry

            lax.fori_loop(0, n_slots, step, 0)

        @pl.when(pl.program_id(0) == 0)
        def _():
            for a in range(n_targets):
                cols = slice(a * width, (a + 1) * width)

                def fix(i, acc, a=a):
                    fix_re, fix_im = acc
                    w = ok_ref[a * n_slots + i].astype(jnp.float32)
                    lr, li, rr, ri = operands(a, i, slice(0, 8))
                    cross = li * ri
                    return (fix_re + w * cross, fix_im + w * (cross - lr * ri - li * rr))

                zero = jnp.zeros((8, width), jnp.float32)
                fix_re, fix_im = lax.fori_loop(0, n_slots, fix, (zero, zero))
                out_re[0:1, cols] += fix_re[0:1]
                out_im[0:1, cols] += fix_im[0:1]

    seg_cols = seg2d.shape[1]
    span_cols = span2d.shape[1]
    grid_spec = pltpu.PrefetchScalarGridSpec(
        num_scalar_prefetch=2,
        grid=(steps,),
        in_specs=[
            pl.BlockSpec((kt, seg_cols), lambda i, l, o: (i, 0)),
            pl.BlockSpec((kt, seg_cols), lambda i, l, o: (i + steps, 0)),
            pl.BlockSpec((kt, span_cols), lambda i, l, o: (i, 0)),
            pl.BlockSpec((kt, span_cols), lambda i, l, o: (i + steps, 0)),
        ],
        out_specs=[
            pl.BlockSpec((kt, n_targets * width), lambda i, l, o: (i, 0)),
            pl.BlockSpec((kt, n_targets * width), lambda i, l, o: (i, 0)),
        ],
    )
    out_shape = [jax.ShapeDtypeStruct((half, n_targets * width), jnp.float32)] * 2
    re, im = pl.pallas_call(kernel, grid_spec=grid_spec, out_shape=out_shape)(
        lag_idx, lag_ok, seg2d, seg2d, span2d, span2d)
    return jnp.concatenate([re, im], axis=0)


def swap(x, axis):
    count = lax.axis_size(axis)
    return lax.ppermute(x, axis, [(i, (i + 1) % count) for i in range(count)])


def layer(
    gate_act, key_act, value_act, filter_taps, skip_gain, w_out, span_order, decode_order
):
    width = gate_act.shape[1]
    length = 2 * SPAN
    cycle_size = lax.axis_size("ctx")
    position = lax.axis_index("ctx")
    count_spans = 2 * cycle_size
    count_lags = 3 * cycle_size
    forward = forward_table(length).astype(jnp.bfloat16)
    inverse = inverse_table(length)
    signal = (key_act.astype(jnp.float32) * value_act.astype(jnp.float32)).astype(jnp.bfloat16)

    own = jnp.concatenate([filter_taps.astype(jnp.bfloat16), signal], axis=0)
    parts = [own] + [
        lax.ppermute(own, "ctx", [(i, (i + shift) % cycle_size) for i in range(cycle_size)])
        for shift in range(1, cycle_size)
    ]
    stacked = jnp.stack(parts)
    tap_rows = filter_taps.shape[0]
    per_lag = tap_rows // SPAN
    per_span = signal.shape[0] // SPAN
    blocks = stacked[:, :tap_rows].reshape(cycle_size, per_lag, SPAN, width)
    piece = stacked[:, tap_rows:].reshape(cycle_size, per_span, SPAN, width)

    previous = jnp.roll(blocks[:, per_lag - 1 :], -1, axis=0)
    first_part = (jnp.arange(cycle_size) == position)[:, None, None, None]
    previous = jnp.where(first_part, jnp.zeros_like(previous), previous)
    earlier = jnp.concatenate([previous, blocks[:, : per_lag - 1]], axis=1)
    seg_time = jnp.concatenate(
        [
            blocks.transpose(2, 0, 1, 3),
            jnp.zeros((1, cycle_size, per_lag, width), jnp.bfloat16),
            earlier[:, :, 1:].transpose(2, 0, 1, 3),
        ],
        axis=0,
    ).reshape(length, count_lags * width)
    seg_spec = jnp.dot(forward, seg_time, preferred_element_type=jnp.float32)
    span_time = piece.transpose(2, 0, 1, 3).reshape(SPAN, count_spans * width)
    span_spec = jnp.dot(forward[:, :SPAN], span_time, preferred_element_type=jnp.float32)

    held = jnp.arange(count_spans)
    global_slot = per_span * ((position - held // per_span) % cycle_size) + held % per_span
    held_spans = span_order[global_slot]
    my_spans = lax.dynamic_slice_in_dim(span_order, per_span * position, per_span)
    my_future = count_spans + lax.dynamic_index_in_dim(decode_order, position, keepdims=False)
    targets = jnp.concatenate([my_spans, my_future[None]])
    lags = targets[:, None] - held_spans[None, :]
    valid = (lags >= 0).astype(jnp.int32)
    lag = jnp.maximum(lags, 0)
    column = per_lag * ((position - lag // per_lag) % cycle_size) + lag % per_lag
    totals = products(seg_spec, span_spec, column[:2].reshape(-1), valid[:2].reshape(-1), 2, width)
    blocks_out = jnp.dot(inverse, totals, precision=HIGH, preferred_element_type=jnp.float32)
    conv = jnp.concatenate([blocks_out[:, :width], blocks_out[:, width:]], axis=0)
    tail_totals = products(seg_spec, span_spec, column[2], valid[2], 1, width)
    tail_inverse, tail_totals = lax.optimization_barrier((inverse, tail_totals))
    tail = jnp.dot(tail_inverse, tail_totals, precision=HIGH, preferred_element_type=jnp.float32)
    mixed = (
        gate_act.astype(jnp.float32) * (conv + skip_gain[None, :] * signal.astype(jnp.float32))
    ).astype(jnp.bfloat16)

    count_z = lax.axis_size("z")
    xlo = lax.axis_index("xlo")
    core = lax.axis_index("core")
    w5 = w_out.reshape(count_z, 2, 2, width, w_out.shape[1])
    rows = count_z * 2 * width
    w_own = lax.dynamic_index_in_dim(w5, core, axis=2, keepdims=False).reshape(rows, -1)
    w_other = lax.dynamic_index_in_dim(w5, 1 - core, axis=2, keepdims=False).reshape(rows, -1)

    other = swap(mixed, "xlo")
    pair = jnp.where(
        xlo == 0,
        jnp.concatenate([mixed, other], axis=1),
        jnp.concatenate([other, mixed], axis=1),
    )
    ring = lax.all_gather(pair, "z", axis=1, tiled=True)
    summed = jnp.dot(ring, w_own, preferred_element_type=jnp.float32) + jnp.dot(
        swap(ring, "core"), w_other, preferred_element_type=jnp.float32
    )
    projected = summed.astype(jnp.bfloat16)
    return (projected, tail)


def solution(mesh):
    ch = mesh.shape["ch"]
    fine = Mesh(
        mesh.devices.reshape(mesh.shape["ctx"], ch // 4, 2, 2), ("ctx", "z", "xlo", "core")
    )
    chans = ("z", "xlo", "core")
    in_specs = (
        P("ctx", chans),
        P("ctx", chans),
        P("ctx", chans),
        P("ctx", chans),
        P(chans),
        P(None, chans),
        P(),
        P(),
    )
    out_specs = (P("ctx", chans), P("ctx", chans))
    return jax.shard_map(layer, mesh=fine, in_specs=in_specs, out_specs=out_specs, check_vma=False)
```

```python
import math

import jax
import jax.numpy as jnp
from jax import lax
from jax.experimental import pallas as pl
from jax.experimental.pallas import tpu as pltpu
from jax.sharding import Mesh, PartitionSpec as P


SPAN = 256

HIGH = lax.Precision.HIGH


def forward_table(length):
    half = length // 2
    rows_idx = lax.broadcasted_iota(jnp.int32, (length, length), 0)
    cols_idx = lax.broadcasted_iota(jnp.int32, (length, length), 1)
    frequency = rows_idx % half
    phase = (frequency * cols_idx % length).astype(jnp.float32) * (2.0 * math.pi / length)
    parity = (1 - 2 * (cols_idx % 2)).astype(jnp.float32)
    table = jnp.where(rows_idx < half, jnp.cos(phase), -jnp.sin(phase))
    return jnp.where(rows_idx == half, parity, table)


def inverse_table(length):
    half = length // 2
    rows_idx = lax.broadcasted_iota(jnp.int32, (half, length), 0)
    cols_idx = lax.broadcasted_iota(jnp.int32, (half, length), 1)
    frequency = cols_idx % half
    phase = (frequency * rows_idx % length).astype(jnp.float32) * (2.0 * math.pi / length)
    weight = jnp.where(frequency == 0, 1.0 / length, 2.0 / length)
    table = jnp.where(cols_idx < half, weight * jnp.cos(phase), -weight * jnp.sin(phase))
    parity = (1 - 2 * (rows_idx % 2)).astype(jnp.float32) / length
    return jnp.where(cols_idx == half, parity, table)


def products(seg2d, span2d, lag_idx, lag_ok, n_targets, width, kt=32):
    half = seg2d.shape[0] // 2
    n_slots = span2d.shape[1] // width
    steps = half // kt

    def kernel(lag_ref, ok_ref, seg_re, seg_im, sp_re, sp_im, out_re, out_im):
        out_re[...] = jnp.zeros_like(out_re)
        out_im[...] = jnp.zeros_like(out_im)

        def operands(a, i, rows):
            off = pl.multiple_of(lag_ref[a * n_slots + i] * width, width)
            own = pl.multiple_of(i * width, width)
            return (
                seg_re[rows, pl.ds(off, width)].astype(jnp.float32),
                seg_im[rows, pl.ds(off, width)].astype(jnp.float32),
                sp_re[rows, pl.ds(own, width)].astype(jnp.float32),
                sp_im[rows, pl.ds(own, width)].astype(jnp.float32),
            )

        for a in range(n_targets):
            cols = slice(a * width, (a + 1) * width)

            def step(i, carry, a=a, cols=cols):
                @pl.when(ok_ref[a * n_slots + i] > 0)
                def _():
                    lr, li, rr, ri = operands(a, i, slice(None))
                    out_re[:, cols] += lr * rr - li * ri
                    out_im[:, cols] += lr * ri + li * rr

                return carry

            lax.fori_loop(0, n_slots, step, 0)

        @pl.when(pl.program_id(0) == 0)
        def _():
            for a in range(n_targets):
                cols = slice(a * width, (a + 1) * width)

                def fix(i, acc, a=a):
                    fix_re, fix_im = acc
                    w = ok_ref[a * n_slots + i].astype(jnp.float32)
                    lr, li, rr, ri = operands(a, i, slice(0, 16))
                    cross = li * ri
                    return (fix_re + w * cross, fix_im + w * (cross - lr * ri - li * rr))

                zero = jnp.zeros((16, width), jnp.float32)
                fix_re, fix_im = lax.fori_loop(0, n_slots, fix, (zero, zero))
                out_re[0:1, cols] += fix_re[0:1]
                out_im[0:1, cols] += fix_im[0:1]

    seg_cols = seg2d.shape[1]
    span_cols = span2d.shape[1]
    grid_spec = pltpu.PrefetchScalarGridSpec(
        num_scalar_prefetch=2,
        grid=(steps,),
        in_specs=[
            pl.BlockSpec((kt, seg_cols), lambda i, l, o: (i, 0)),
            pl.BlockSpec((kt, seg_cols), lambda i, l, o: (i + steps, 0)),
            pl.BlockSpec((kt, span_cols), lambda i, l, o: (i, 0)),
            pl.BlockSpec((kt, span_cols), lambda i, l, o: (i + steps, 0)),
        ],
        out_specs=[
            pl.BlockSpec((kt, n_targets * width), lambda i, l, o: (i, 0)),
            pl.BlockSpec((kt, n_targets * width), lambda i, l, o: (i, 0)),
        ],
    )
    out_shape = [jax.ShapeDtypeStruct((half, n_targets * width), jnp.float32)] * 2
    re, im = pl.pallas_call(kernel, grid_spec=grid_spec, out_shape=out_shape)(
        lag_idx, lag_ok, seg2d, seg2d, span2d, span2d)
    return jnp.concatenate([re, im], axis=0)


def swap(x, axis):
    count = lax.axis_size(axis)
    return lax.ppermute(x, axis, [(i, (i + 1) % count) for i in range(count)])


def layer(
    gate_act, key_act, value_act, filter_taps, skip_gain, w_out, span_order, decode_order
):
    width = gate_act.shape[1]
    length = 2 * SPAN
    cycle_size = lax.axis_size("ctx")
    position = lax.axis_index("ctx")
    count_spans = 2 * cycle_size
    count_lags = 3 * cycle_size
    forward = forward_table(length).astype(jnp.bfloat16)
    inverse = inverse_table(length)
    signal = (key_act.astype(jnp.float32) * value_act.astype(jnp.float32)).astype(jnp.bfloat16)

    own = jnp.concatenate([filter_taps.astype(jnp.bfloat16), signal], axis=0)
    parts = [own] + [
        lax.ppermute(own, "ctx", [(i, (i + shift) % cycle_size) for i in range(cycle_size)])
        for shift in range(1, cycle_size)
    ]
    stacked = jnp.stack(parts)
    tap_rows = filter_taps.shape[0]
    per_lag = tap_rows // SPAN
    per_span = signal.shape[0] // SPAN
    blocks = stacked[:, :tap_rows].reshape(cycle_size, per_lag, SPAN, width)
    piece = stacked[:, tap_rows:].reshape(cycle_size, per_span, SPAN, width)

    previous = jnp.roll(blocks[:, per_lag - 1 :], -1, axis=0)
    first_part = (jnp.arange(cycle_size) == position)[:, None, None, None]
    previous = jnp.where(first_part, jnp.zeros_like(previous), previous)
    earlier = jnp.concatenate([previous, blocks[:, : per_lag - 1]], axis=1)
    seg_time = jnp.concatenate(
        [
            blocks.transpose(2, 0, 1, 3),
            jnp.zeros((1, cycle_size, per_lag, width), jnp.bfloat16),
            earlier[:, :, 1:].transpose(2, 0, 1, 3),
        ],
        axis=0,
    ).reshape(length, count_lags * width)
    seg_spec = jnp.dot(forward, seg_time, preferred_element_type=jnp.float32).astype(jnp.bfloat16)
    span_time = piece.transpose(2, 0, 1, 3).reshape(SPAN, count_spans * width)
    span_spec = jnp.dot(
        forward[:, :SPAN], span_time, preferred_element_type=jnp.float32
    ).astype(jnp.bfloat16)

    held = jnp.arange(count_spans)
    global_slot = per_span * ((position - held // per_span) % cycle_size) + held % per_span
    held_spans = span_order[global_slot]
    my_spans = lax.dynamic_slice_in_dim(span_order, per_span * position, per_span)
    my_future = count_spans + lax.dynamic_index_in_dim(decode_order, position, keepdims=False)
    targets = jnp.concatenate([my_spans, my_future[None]])
    lags = targets[:, None] - held_spans[None, :]
    valid = (lags >= 0).astype(jnp.int32)
    lag = jnp.maximum(lags, 0)
    column = per_lag * ((position - lag // per_lag) % cycle_size) + lag % per_lag
    totals = products(seg_spec, span_spec, column[:2].reshape(-1), valid[:2].reshape(-1), 2, width)
    blocks_out = jnp.dot(inverse, totals, precision=HIGH, preferred_element_type=jnp.float32)
    conv = jnp.concatenate([blocks_out[:, :width], blocks_out[:, width:]], axis=0)
    tail_totals = products(seg_spec, span_spec, column[2], valid[2], 1, width)
    tail_inverse, tail_totals = lax.optimization_barrier((inverse, tail_totals))
    tail = jnp.dot(tail_inverse, tail_totals, precision=HIGH, preferred_element_type=jnp.float32)
    mixed = (
        gate_act.astype(jnp.float32) * (conv + skip_gain[None, :] * signal.astype(jnp.float32))
    ).astype(jnp.bfloat16)

    count_z = lax.axis_size("z")
    core = lax.axis_index("core")
    w5 = w_out.reshape(count_z, 2, 2, width, w_out.shape[1])
    rows = count_z * 2 * width
    w_own = lax.dynamic_index_in_dim(w5, core, axis=2, keepdims=False).reshape(rows, -1)
    w_other = lax.dynamic_index_in_dim(w5, 1 - core, axis=2, keepdims=False).reshape(rows, -1)

    ring = lax.all_gather(mixed, ("z", "xlo"), axis=1, tiled=True)
    summed = jnp.dot(ring, w_own, preferred_element_type=jnp.float32) + jnp.dot(
        swap(ring, "core"), w_other, preferred_element_type=jnp.float32
    )
    projected = summed.astype(jnp.bfloat16)
    return (projected, tail)


def solution(mesh):
    ch = mesh.shape["ch"]
    fine = Mesh(
        mesh.devices.reshape(mesh.shape["ctx"], ch // 4, 2, 2), ("ctx", "z", "xlo", "core")
    )
    chans = ("z", "xlo", "core")
    in_specs = (
        P("ctx", chans),
        P("ctx", chans),
        P("ctx", chans),
        P("ctx", chans),
        P(chans),
        P(None, chans),
        P(),
        P(),
    )
    out_specs = (P("ctx", chans), P("ctx", chans))
    return jax.shard_map(layer, mesh=fine, in_specs=in_specs, out_specs=out_specs, check_vma=False)
```

```python
import math

import jax
import jax.numpy as jnp
from jax import lax
from jax.experimental import pallas as pl
from jax.experimental.pallas import tpu as pltpu
from jax.sharding import Mesh, PartitionSpec as P


SPAN = 256


HIGH = lax.Precision.HIGH


def forward_table(length):
    half = length // 2
    rows_idx = lax.broadcasted_iota(jnp.int32, (length, length), 0)
    cols_idx = lax.broadcasted_iota(jnp.int32, (length, length), 1)
    frequency = rows_idx % half
    phase = (frequency * cols_idx % length).astype(jnp.float32) * (2.0 * math.pi / length)
    parity = (1 - 2 * (cols_idx % 2)).astype(jnp.float32)
    table = jnp.where(rows_idx < half, jnp.cos(phase), -jnp.sin(phase))
    return jnp.where(rows_idx == half, parity, table)


def inverse_table(length):
    half = length // 2
    rows_idx = lax.broadcasted_iota(jnp.int32, (half, length), 0)
    cols_idx = lax.broadcasted_iota(jnp.int32, (half, length), 1)
    frequency = cols_idx % half
    phase = (frequency * rows_idx % length).astype(jnp.float32) * (2.0 * math.pi / length)
    weight = jnp.where(frequency == 0, 1.0 / length, 2.0 / length)
    table = jnp.where(cols_idx < half, weight * jnp.cos(phase), -weight * jnp.sin(phase))
    parity = (1 - 2 * (rows_idx % 2)).astype(jnp.float32) / length
    return jnp.where(cols_idx == half, parity, table)


def products(seg2d, span2d, lag_idx, lag_ok, n_targets, width, kt=32):
    half = seg2d.shape[0] // 2
    n_slots = span2d.shape[1] // width
    steps = half // kt

    def kernel(lag_ref, ok_ref, seg_re, seg_im, sp_re, sp_im, out_re, out_im):
        out_re[...] = jnp.zeros_like(out_re)
        out_im[...] = jnp.zeros_like(out_im)

        def operands(a, i, rows):
            off = pl.multiple_of(lag_ref[a * n_slots + i] * width, width)
            own = pl.multiple_of(i * width, width)
            return (
                seg_re[rows, pl.ds(off, width)].astype(jnp.float32),
                seg_im[rows, pl.ds(off, width)].astype(jnp.float32),
                sp_re[rows, pl.ds(own, width)].astype(jnp.float32),
                sp_im[rows, pl.ds(own, width)].astype(jnp.float32),
            )

        for a in range(n_targets):
            cols = slice(a * width, (a + 1) * width)

            def step(i, carry, a=a, cols=cols):
                @pl.when(ok_ref[a * n_slots + i] > 0)
                def _():
                    lr, li, rr, ri = operands(a, i, slice(None))
                    out_re[:, cols] += lr * rr - li * ri
                    out_im[:, cols] += lr * ri + li * rr

                return carry

            lax.fori_loop(0, n_slots, step, 0)

        @pl.when(pl.program_id(0) == 0)
        def _():
            for a in range(n_targets):
                cols = slice(a * width, (a + 1) * width)

                def fix(i, acc, a=a):
                    fix_re, fix_im = acc
                    w = ok_ref[a * n_slots + i].astype(jnp.float32)
                    lr, li, rr, ri = operands(a, i, slice(0, 16))
                    cross = li * ri
                    return (fix_re + w * cross, fix_im + w * (cross - lr * ri - li * rr))

                zero = jnp.zeros((16, width), jnp.float32)
                fix_re, fix_im = lax.fori_loop(0, n_slots, fix, (zero, zero))
                out_re[0:1, cols] += fix_re[0:1]
                out_im[0:1, cols] += fix_im[0:1]

    seg_cols = seg2d.shape[1]
    span_cols = span2d.shape[1]
    grid_spec = pltpu.PrefetchScalarGridSpec(
        num_scalar_prefetch=2,
        grid=(steps,),
        in_specs=[
            pl.BlockSpec((kt, seg_cols), lambda i, l, o: (i, 0)),
            pl.BlockSpec((kt, seg_cols), lambda i, l, o: (i + steps, 0)),
            pl.BlockSpec((kt, span_cols), lambda i, l, o: (i, 0)),
            pl.BlockSpec((kt, span_cols), lambda i, l, o: (i + steps, 0)),
        ],
        out_specs=[
            pl.BlockSpec((kt, n_targets * width), lambda i, l, o: (i, 0)),
            pl.BlockSpec((kt, n_targets * width), lambda i, l, o: (i, 0)),
        ],
    )
    out_shape = [jax.ShapeDtypeStruct((half, n_targets * width), jnp.float32)] * 2
    re, im = pl.pallas_call(kernel, grid_spec=grid_spec, out_shape=out_shape)(
        lag_idx, lag_ok, seg2d, seg2d, span2d, span2d)
    return jnp.concatenate([re, im], axis=0)


def swap(x, axis):
    count = lax.axis_size(axis)
    return lax.ppermute(x, axis, [(i, (i + 1) % count) for i in range(count)])


def layer(
    gate_act, key_act, value_act, filter_taps, skip_gain, w_out, span_order, decode_order
):
    width = gate_act.shape[1]
    length = 2 * SPAN
    cycle_size = lax.axis_size("ctx")
    position = lax.axis_index("ctx")
    count_spans = 2 * cycle_size
    count_lags = 3 * cycle_size
    forward = forward_table(length).astype(jnp.bfloat16)
    inverse = inverse_table(length)
    signal = (key_act.astype(jnp.float32) * value_act.astype(jnp.float32)).astype(jnp.bfloat16)

    own = jnp.concatenate([filter_taps.astype(jnp.bfloat16), signal], axis=0)
    parts = [own] + [
        lax.ppermute(own, "ctx", [(i, (i + shift) % cycle_size) for i in range(cycle_size)])
        for shift in range(1, cycle_size)
    ]
    stacked = jnp.stack(parts)
    tap_rows = filter_taps.shape[0]
    per_lag = tap_rows // SPAN
    per_span = signal.shape[0] // SPAN
    blocks = stacked[:, :tap_rows].reshape(cycle_size, per_lag, SPAN, width)
    piece = stacked[:, tap_rows:].reshape(cycle_size, per_span, SPAN, width)

    previous = jnp.roll(blocks[:, per_lag - 1 :], -1, axis=0)
    first_part = (jnp.arange(cycle_size) == position)[:, None, None, None]
    previous = jnp.where(first_part, jnp.zeros_like(previous), previous)
    earlier = jnp.concatenate([previous, blocks[:, : per_lag - 1]], axis=1)
    seg_time = jnp.concatenate(
        [
            blocks.transpose(2, 0, 1, 3),
            jnp.zeros((1, cycle_size, per_lag, width), jnp.bfloat16),
            earlier[:, :, 1:].transpose(2, 0, 1, 3),
        ],
        axis=0,
    ).reshape(length, count_lags * width)
    seg_spec = jnp.dot(forward, seg_time, preferred_element_type=jnp.float32).astype(jnp.bfloat16)
    span_time = piece.transpose(2, 0, 1, 3).reshape(SPAN, count_spans * width)
    span_spec = jnp.dot(
        forward[:, :SPAN], span_time, preferred_element_type=jnp.float32
    ).astype(jnp.bfloat16)

    held = jnp.arange(count_spans)
    global_slot = per_span * ((position - held // per_span) % cycle_size) + held % per_span
    held_spans = span_order[global_slot]
    my_spans = lax.dynamic_slice_in_dim(span_order, per_span * position, per_span)
    my_future = count_spans + lax.dynamic_index_in_dim(decode_order, position, keepdims=False)
    targets = jnp.concatenate([my_spans, my_future[None]])
    lags = targets[:, None] - held_spans[None, :]
    valid = (lags >= 0).astype(jnp.int32)
    lag = jnp.maximum(lags, 0)
    column = per_lag * ((position - lag // per_lag) % cycle_size) + lag % per_lag
    totals = products(seg_spec, span_spec, column[:2].reshape(-1), valid[:2].reshape(-1), 2, width)
    blocks_out = jnp.dot(inverse, totals, precision=HIGH, preferred_element_type=jnp.float32)
    conv = jnp.concatenate([blocks_out[:, :width], blocks_out[:, width:]], axis=0)
    tail_totals = products(seg_spec, span_spec, column[2], valid[2], 1, width)
    tail_inverse, tail_totals = lax.optimization_barrier((inverse, tail_totals))
    tail = jnp.dot(tail_inverse, tail_totals, precision=HIGH, preferred_element_type=jnp.float32)
    mixed = (
        gate_act.astype(jnp.float32) * (conv + skip_gain[None, :] * signal.astype(jnp.float32))
    ).astype(jnp.bfloat16)

    count_z = lax.axis_size("z")
    xlo = lax.axis_index("xlo")
    core = lax.axis_index("core")
    w5 = w_out.reshape(count_z, 2, 2, width, w_out.shape[1])
    rows = count_z * 2 * width
    w_own = lax.dynamic_index_in_dim(w5, core, axis=2, keepdims=False).reshape(rows, -1)
    w_other = lax.dynamic_index_in_dim(w5, 1 - core, axis=2, keepdims=False).reshape(rows, -1)

    other = swap(mixed, "xlo")
    pair = jnp.where(
        xlo == 0,
        jnp.concatenate([mixed, other], axis=1),
        jnp.concatenate([other, mixed], axis=1),
    )
    ring = lax.all_gather(pair, "z", axis=1, tiled=True)
    summed = jnp.dot(ring, w_own, preferred_element_type=jnp.float32) + jnp.dot(
        swap(ring, "core"), w_other, preferred_element_type=jnp.float32
    )
    projected = summed.astype(jnp.bfloat16)
    return (projected, tail)


def solution(mesh):
    ch = mesh.shape["ch"]
    fine = Mesh(
        mesh.devices.reshape(mesh.shape["ctx"], ch // 4, 2, 2), ("ctx", "z", "xlo", "core")
    )
    chans = ("z", "xlo", "core")
    in_specs = (
        P("ctx", chans),
        P("ctx", chans),
        P("ctx", chans),
        P("ctx", chans),
        P(chans),
        P(None, chans),
        P(),
        P(),
    )
    out_specs = (P("ctx", chans), P("ctx", chans))
    return jax.shard_map(layer, mesh=fine, in_specs=in_specs, out_specs=out_specs, check_vma=False)
```

```python
import math

import jax
import jax.numpy as jnp
from jax import lax
from jax.experimental import pallas as pl
from jax.experimental.pallas import tpu as pltpu
from jax.sharding import Mesh, PartitionSpec as P


SPAN = 256


HIGH = lax.Precision.HIGH


def forward_table(length):
    half = length // 2
    rows_idx = lax.broadcasted_iota(jnp.int32, (length, length), 0)
    cols_idx = lax.broadcasted_iota(jnp.int32, (length, length), 1)
    frequency = rows_idx % half
    phase = (frequency * cols_idx % length).astype(jnp.float32) * (2.0 * math.pi / length)
    parity = (1 - 2 * (cols_idx % 2)).astype(jnp.float32)
    table = jnp.where(rows_idx < half, jnp.cos(phase), -jnp.sin(phase))
    return jnp.where(rows_idx == half, parity, table)


def inverse_table(length):
    half = length // 2
    rows_idx = lax.broadcasted_iota(jnp.int32, (half, length), 0)
    cols_idx = lax.broadcasted_iota(jnp.int32, (half, length), 1)
    frequency = cols_idx % half
    phase = (frequency * rows_idx % length).astype(jnp.float32) * (2.0 * math.pi / length)
    weight = jnp.where(frequency == 0, 1.0 / length, 2.0 / length)
    table = jnp.where(cols_idx < half, weight * jnp.cos(phase), -weight * jnp.sin(phase))
    parity = (1 - 2 * (rows_idx % 2)).astype(jnp.float32) / length
    return jnp.where(cols_idx == half, parity, table)


def products(seg2d, span2d, lag_idx, lag_ok, n_targets, width, kt=128):
    half = seg2d.shape[0] // 2
    n_slots = span2d.shape[1] // width
    steps = half // kt

    def kernel(lag_ref, ok_ref, seg_re, seg_im, sp_re, sp_im, out_re, out_im):
        out_re[...] = jnp.zeros_like(out_re)
        out_im[...] = jnp.zeros_like(out_im)

        def operands(a, i, rows):
            off = pl.multiple_of(lag_ref[a * n_slots + i] * width, width)
            own = pl.multiple_of(i * width, width)
            return (
                seg_re[rows, pl.ds(off, width)].astype(jnp.float32),
                seg_im[rows, pl.ds(off, width)].astype(jnp.float32),
                sp_re[rows, pl.ds(own, width)].astype(jnp.float32),
                sp_im[rows, pl.ds(own, width)].astype(jnp.float32),
            )

        for a in range(n_targets):
            cols = slice(a * width, (a + 1) * width)

            def step(i, carry, a=a, cols=cols):
                @pl.when(ok_ref[a * n_slots + i] > 0)
                def _():
                    lr, li, rr, ri = operands(a, i, slice(None))
                    out_re[:, cols] += lr * rr - li * ri
                    out_im[:, cols] += lr * ri + li * rr

                return carry

            lax.fori_loop(0, n_slots, step, 0)

        @pl.when(pl.program_id(0) == 0)
        def _():
            for a in range(n_targets):
                cols = slice(a * width, (a + 1) * width)

                def fix(i, acc, a=a):
                    fix_re, fix_im = acc
                    w = ok_ref[a * n_slots + i].astype(jnp.float32)
                    lr, li, rr, ri = operands(a, i, slice(0, 16))
                    cross = li * ri
                    return (fix_re + w * cross, fix_im + w * (cross - lr * ri - li * rr))

                zero = jnp.zeros((16, width), jnp.float32)
                fix_re, fix_im = lax.fori_loop(0, n_slots, fix, (zero, zero))
                out_re[0:1, cols] += fix_re[0:1]
                out_im[0:1, cols] += fix_im[0:1]

    seg_cols = seg2d.shape[1]
    span_cols = span2d.shape[1]
    grid_spec = pltpu.PrefetchScalarGridSpec(
        num_scalar_prefetch=2,
        grid=(steps,),
        in_specs=[
            pl.BlockSpec((kt, seg_cols), lambda i, l, o: (i, 0)),
            pl.BlockSpec((kt, seg_cols), lambda i, l, o: (i + steps, 0)),
            pl.BlockSpec((kt, span_cols), lambda i, l, o: (i, 0)),
            pl.BlockSpec((kt, span_cols), lambda i, l, o: (i + steps, 0)),
        ],
        out_specs=[
            pl.BlockSpec((kt, n_targets * width), lambda i, l, o: (i, 0)),
            pl.BlockSpec((kt, n_targets * width), lambda i, l, o: (i, 0)),
        ],
    )
    out_shape = [jax.ShapeDtypeStruct((half, n_targets * width), jnp.float32)] * 2
    re, im = pl.pallas_call(kernel, grid_spec=grid_spec, out_shape=out_shape)(
        lag_idx, lag_ok, seg2d, seg2d, span2d, span2d)
    return jnp.concatenate([re, im], axis=0)


def swap(x, axis):
    count = lax.axis_size(axis)
    return lax.ppermute(x, axis, [(i, (i + 1) % count) for i in range(count)])


def layer(
    gate_act, key_act, value_act, filter_taps, skip_gain, w_out, span_order, decode_order
):
    width = gate_act.shape[1]
    length = 2 * SPAN
    cycle_size = lax.axis_size("ctx")
    position = lax.axis_index("ctx")
    count_spans = 2 * cycle_size
    count_lags = 3 * cycle_size
    forward = forward_table(length).astype(jnp.bfloat16)
    inverse = inverse_table(length)
    signal = (key_act.astype(jnp.float32) * value_act.astype(jnp.float32)).astype(jnp.bfloat16)

    own = jnp.concatenate([filter_taps.astype(jnp.bfloat16), signal], axis=0)
    parts = [own] + [
        lax.ppermute(own, "ctx", [(i, (i + shift) % cycle_size) for i in range(cycle_size)])
        for shift in range(1, cycle_size)
    ]
    stacked = jnp.stack(parts)
    tap_rows = filter_taps.shape[0]
    per_lag = tap_rows // SPAN
    per_span = signal.shape[0] // SPAN
    blocks = stacked[:, :tap_rows].reshape(cycle_size, per_lag, SPAN, width)
    piece = stacked[:, tap_rows:].reshape(cycle_size, per_span, SPAN, width)

    previous = jnp.roll(blocks[:, per_lag - 1 :], -1, axis=0)
    first_part = (jnp.arange(cycle_size) == position)[:, None, None, None]
    previous = jnp.where(first_part, jnp.zeros_like(previous), previous)
    earlier = jnp.concatenate([previous, blocks[:, : per_lag - 1]], axis=1)
    seg_time = jnp.concatenate(
        [
            blocks.transpose(2, 0, 1, 3),
            jnp.zeros((1, cycle_size, per_lag, width), jnp.bfloat16),
            earlier[:, :, 1:].transpose(2, 0, 1, 3),
        ],
        axis=0,
    ).reshape(length, count_lags * width)
    seg_spec = jnp.dot(forward, seg_time, preferred_element_type=jnp.float32).astype(jnp.bfloat16)
    span_time = piece.transpose(2, 0, 1, 3).reshape(SPAN, count_spans * width)
    span_spec = jnp.dot(
        forward[:, :SPAN], span_time, preferred_element_type=jnp.float32
    ).astype(jnp.bfloat16)

    held = jnp.arange(count_spans)
    global_slot = per_span * ((position - held // per_span) % cycle_size) + held % per_span
    held_spans = span_order[global_slot]
    my_spans = lax.dynamic_slice_in_dim(span_order, per_span * position, per_span)
    my_future = count_spans + lax.dynamic_index_in_dim(decode_order, position, keepdims=False)
    targets = jnp.concatenate([my_spans, my_future[None]])
    lags = targets[:, None] - held_spans[None, :]
    valid = (lags >= 0).astype(jnp.int32)
    lag = jnp.maximum(lags, 0)
    column = per_lag * ((position - lag // per_lag) % cycle_size) + lag % per_lag
    totals = products(seg_spec, span_spec, column[:2].reshape(-1), valid[:2].reshape(-1), 2, width)
    blocks_out = jnp.dot(inverse, totals, precision=HIGH, preferred_element_type=jnp.float32)
    conv = jnp.concatenate([blocks_out[:, :width], blocks_out[:, width:]], axis=0)
    tail_totals = products(seg_spec, span_spec, column[2], valid[2], 1, width)
    tail_inverse, tail_totals = lax.optimization_barrier((inverse, tail_totals))
    tail = jnp.dot(tail_inverse, tail_totals, precision=HIGH, preferred_element_type=jnp.float32)
    mixed = (
        gate_act.astype(jnp.float32) * (conv + skip_gain[None, :] * signal.astype(jnp.float32))
    ).astype(jnp.bfloat16)

    count_z = lax.axis_size("z")
    xlo = lax.axis_index("xlo")
    core = lax.axis_index("core")
    w5 = w_out.reshape(count_z, 2, 2, width, w_out.shape[1])
    rows = count_z * 2 * width
    w_own = lax.dynamic_index_in_dim(w5, core, axis=2, keepdims=False).reshape(rows, -1)
    w_other = lax.dynamic_index_in_dim(w5, 1 - core, axis=2, keepdims=False).reshape(rows, -1)
    w_partner = swap(w_other, "core")

    other = swap(mixed, "xlo")
    pair = jnp.where(
        xlo == 0,
        jnp.concatenate([mixed, other], axis=1),
        jnp.concatenate([other, mixed], axis=1),
    )
    ring = lax.all_gather(pair, "z", axis=1, tiled=True)
    for_partner = jnp.dot(ring, w_partner, preferred_element_type=jnp.float32)
    summed = jnp.dot(ring, w_own, preferred_element_type=jnp.float32) + swap(for_partner, "core")
    projected = summed.astype(jnp.bfloat16)
    return (projected, tail)


def solution(mesh):
    ch = mesh.shape["ch"]
    fine = Mesh(
        mesh.devices.reshape(mesh.shape["ctx"], ch // 4, 2, 2), ("ctx", "z", "xlo", "core")
    )
    chans = ("z", "xlo", "core")
    in_specs = (
        P("ctx", chans),
        P("ctx", chans),
        P("ctx", chans),
        P("ctx", chans),
        P(chans),
        P(None, chans),
        P(),
        P(),
    )
    out_specs = (P("ctx", chans), P("ctx", chans))
    return jax.shard_map(layer, mesh=fine, in_specs=in_specs, out_specs=out_specs, check_vma=False)
```
